256 devices in a mesh: seq: 64 (over x, z, core), head: 4 (over y).
Axes of the slice: x: 4, y: 4, z: 8, core: 2. Of those that a mesh axis runs over, the one named last changes fastest.
Arguments:
- queries: bfloat16 [16384, 2048], P('seq', 'head'), may hold values from -30 to 30, as said below
- keys: bfloat16 [16384, 2048], P('seq', 'head'), may hold values from -30 to 30, as said below
- values: bfloat16 [16384, 2048], P('seq', 'head'), may hold values from -6 to 6
- out_grad: bfloat16 [16384, 2048], P('seq', 'head'), may hold values from -6 to 6
- rand_blocks: int32 [16, 128, 3], P('head', 'seq'), may hold values from 0 to 127, as said below
Outputs:
- attn_out: bfloat16 [16384, 2048], P('seq', 'head')
- grad_queries: bfloat16 [16384, 2048], P('seq', 'head')
- grad_keys: bfloat16 [16384, 2048], P('seq', 'head')
- grad_values: bfloat16 [16384, 2048], P('seq', 'head')
The draws below stay inside these ranges and needn't reach their ends.
Inputs may be any that keep to these rules, and one draw needn't show every extreme that they name: queries are of order one; in some draws a few rows reach larger scales. keys are of order one; in some draws a few rows reach larger scales. `rand_blocks`: for each aligned group of 4 heads and each aligned run of 2 query blocks, at most 2 of the group's entries name blocks of one aligned run of 2 key blocks, and in every group some run is named exactly 2 times.
All inputs are finite; a program needn't handle non-finite values.
Results may differ from the reference program's by a relative error of at most 0.015.
The reference program's roundings to bfloat16 on the way count: a program that leaves them out, or rounds other values in their place, can miss the bound.
Values may be sent and summed in bfloat16 or wider, within the bound.
No kernel may reach another device: no remote copies, remote signals or barrier semaphores. Data moves between devices by JAX's collectives and lax.ppermute only.
A program may use at most 192 MiB of HBM per device.

```python
import math
import jax
import jax.numpy as jnp
from jax import lax

HEADS = 16
DH = 128
BS = 128
RAND = 3
BLK_DEV = 2
NB = 128
SEQ = 16384
HL = 4
CAP = 2
NEAR_BITS = 1
FAR_BITS = 6


def base_pair(key):
    row_count = NB * BS
    row_width = HEADS * DH
    query_base = jnp.clip(jax.random.normal(jax.random.fold_in(key, 11), (row_count, row_width), jnp.float32), -6.0, 6.0)
    key_base = jnp.clip(jax.random.normal(jax.random.fold_in(key, 12), (row_count, row_width), jnp.float32), -6.0, 6.0)
    return (query_base, key_base)


def draw_queries(key, part):
    query_base, key_base = base_pair(key)
    result = query_base
    return result.astype(jnp.bfloat16)


def draw_keys(key, part):
    query_base, key_base = base_pair(key)
    result = key_base
    return result.astype(jnp.bfloat16)


def draw_rand_blocks(key, part):
    seq_groups = NB // BLK_DEV
    head_groups = HEADS // HL
    per_group = HL * BLK_DEV * RAND
    hot_devs = jax.random.permutation(jax.random.fold_in(key, 21), seq_groups) < max(1, seq_groups // 8)

    def one_group(group_key):
        owner_order = jax.random.permutation(jax.random.fold_in(group_key, 1), seq_groups)
        hot_rank = jnp.argsort(jnp.where(hot_devs[owner_order], 0, 1).astype(jnp.int32), stable=True)
        owner_order = owner_order[hot_rank]
        owner_list = jnp.repeat(owner_order, CAP, total_repeat_length=seq_groups * CAP)[:per_group]
        owner_list = owner_list[jax.random.permutation(jax.random.fold_in(group_key, 2), per_group)]
        local_blk = jax.random.randint(jax.random.fold_in(group_key, 3), (per_group,), 0, BLK_DEV)
        return owner_list * BLK_DEV + local_blk
    group_keys = jax.random.split(jax.random.fold_in(key, 20), head_groups * seq_groups)
    flat_ids = jax.vmap(one_group)(group_keys)
    arranged = flat_ids.reshape(head_groups, seq_groups, HL, BLK_DEV, RAND).transpose(0, 2, 1, 3, 4)
    return arranged.reshape(HEADS, NB, RAND).astype(jnp.int32)


def block_levels(stream_key, dims, shards, smallest, top_value):
    def one(axis_at, parts):
        draws = jax.random.uniform(jax.random.fold_in(jax.random.fold_in(stream_key, 6), axis_at), (parts,), jnp.float32, smallest / len(shards), top_value / len(shards))
        return jnp.repeat(jnp.exp(draws), dims[axis_at] // parts).reshape((-1,) + (1,) * (len(dims) - axis_at - 1))

    loudness = one(*shards[0])
    for cut in shards[1:]:
        loudness = loudness * one(*cut)
    return loudness


def normal_values(key, extent, width, limit, pieces=(), held_as=jnp.bfloat16):
    values = width * jax.random.normal(key, extent, jnp.float32)
    if pieces:
        values = values * block_levels(key, extent, pieces, -0.22, 0.18)
    return jnp.clip(values, -limit, limit).astype(held_as)


def setup_inputs(seed: int = 0) -> dict:
    seeds = jax.random.split(jax.random.key(seed), 6)
    queries = draw_queries(jax.random.fold_in(seeds[5], 71), 0)
    keys = draw_keys(jax.random.fold_in(seeds[5], 71), 0)
    values = normal_values(seeds[2], (SEQ, HEADS * DH), 1.0, 6.0, ((0, 64), (1, 4)))
    out_grad = normal_values(seeds[3], (SEQ, HEADS * DH), 1.0, 6.0, ((0, 64), (1, 4)))
    rand_blocks = draw_rand_blocks(jax.random.fold_in(seeds[5], 71), 0)
    return {"queries": queries, "keys": keys, "values": values, "out_grad": out_grad, "rand_blocks": rand_blocks}


def round_trip(value_arr):
    return lax.optimization_barrier(value_arr.astype(jnp.bfloat16)).astype(jnp.float32)

def reference(queries, keys, values, out_grad, rand_blocks):
    score_scale = 1.0 / math.sqrt(DH)
    bit_count = NEAR_BITS + FAR_BITS
    block_ids = jnp.arange(NB, dtype=jnp.int32)
    fixed_cols = [block_ids] + [jnp.bitwise_xor(block_ids, jnp.int32(1 << bit_pos)) for bit_pos in range(bit_count)]
    fixed_index = jnp.stack(fixed_cols, axis=1)

    def by_head(array_in):
        return array_in.reshape(NB, BS, HEADS, DH).transpose(2, 0, 1, 3)

    def one_head(head_items):
        query_rows, key_rows, value_rows, grad_rows, rand_rows = head_items
        key_index = jnp.concatenate([fixed_index, rand_rows.astype(jnp.int32)], axis=1)
        key_set = key_rows[key_index].astype(jnp.float32)
        value_set = value_rows[key_index].astype(jnp.float32)
        query_wide = query_rows.astype(jnp.float32)
        grad_wide = grad_rows.astype(jnp.float32)
        scores = jnp.einsum('btd,bksd->btks', query_wide, key_set) * score_scale
        row_max = lax.optimization_barrier(jnp.max(scores, axis=(2, 3)))
        log_total = row_max + jnp.log(lax.optimization_barrier(jnp.sum(jnp.exp(scores - row_max[:, :, None, None]), axis=(2, 3))))
        weights = jnp.exp(scores - log_total[:, :, None, None])
        weights_low = round_trip(weights)
        attn_rows = jnp.einsum('btks,bksd->btd', weights_low, value_set).astype(jnp.bfloat16)
        attn_wide = lax.optimization_barrier(attn_rows).astype(jnp.float32)
        row_delta = lax.optimization_barrier(jnp.sum(grad_wide * attn_wide, axis=2))
        grad_weights = jnp.einsum('btd,bksd->btks', grad_wide, value_set)
        grad_scores = round_trip(weights * (grad_weights - row_delta[:, :, None, None]))
        grad_query = (score_scale * jnp.einsum('btks,bksd->btd', grad_scores, key_set)).astype(jnp.bfloat16)
        key_terms = score_scale * jnp.einsum('btks,btd->bksd', grad_scores, query_wide)
        value_terms = jnp.einsum('btks,btd->bksd', weights_low, grad_wide)
        zero_rows = jnp.zeros((NB, BS, DH), jnp.float32)
        grad_key = key_terms[:, 0] + zero_rows.at[key_index[:, 1:]].add(round_trip(key_terms[:, 1:]))
        grad_value = value_terms[:, 0] + zero_rows.at[key_index[:, 1:]].add(round_trip(value_terms[:, 1:]))
        return (attn_rows, grad_query, grad_key.astype(jnp.bfloat16), grad_value.astype(jnp.bfloat16))
    results = lax.map(one_head, (by_head(queries), by_head(keys), by_head(values), by_head(out_grad), rand_blocks))

    def back_rows(array_in):
        return array_in.transpose(1, 2, 0, 3).reshape(NB * BS, HEADS * DH)
    return (back_rows(results[0]), back_rows(results[1]), back_rows(results[2]), back_rows(results[3]))
```

```python
import math

import jax
import jax.numpy as jnp
from jax import lax
from jax.sharding import PartitionSpec as P


def swapped(value, axis, distance):
    mask = 2**distance
    pairs = [(source, source ^ mask) for source in range(lax.axis_size(axis))]
    return lax.ppermute(value, axis, pairs)


def low(value_arr):
    return value_arr.astype(jnp.bfloat16).astype(jnp.float32)


def local(queries, keys, values, out_grad, rand_blocks):
    tok_rows = queries.shape[0]
    heads_here, blk_count, rand_count = rand_blocks.shape
    head_size = queries.shape[1] // heads_here
    blk_size = tok_rows // blk_count
    score_scale = 1.0 / math.sqrt(head_size)
    seq_devices = lax.axis_size("seq")
    far_count = seq_devices.bit_length() - 1
    f32 = jnp.float32

    def heads_first(arr):
        return arr.reshape(blk_count, blk_size, heads_here, head_size).transpose(2, 0, 1, 3)

    def rows_back(arr):
        return arr.transpose(1, 2, 0, 3).reshape(tok_rows, heads_here * head_size)

    total_req = heads_here * blk_count * rand_count
    slot_cap = max(2, -(-total_req // seq_devices))
    slot_count = seq_devices * slot_cap
    flat_req = rand_blocks.reshape(-1)
    owner_dev = flat_req // blk_count
    req_index = jnp.arange(total_req, dtype=jnp.int32)
    req_head = req_index // (blk_count * rand_count)
    payload = req_head * blk_count + flat_req % blk_count
    earlier_same = (owner_dev[:, None] == owner_dev[None, :]) & (
        req_index[:, None] > req_index[None, :]
    )
    slot_rank = jnp.sum(earlier_same.astype(jnp.int32), axis=1)
    slot_of_req = owner_dev * slot_cap + slot_rank
    slot_match = slot_of_req[None, :] == jnp.arange(slot_count, dtype=jnp.int32)[:, None]
    filled = jnp.any(slot_match, axis=1)
    send_ids = jnp.where(filled, jnp.sum(jnp.where(slot_match, payload[None, :], 0), axis=1), -1)
    asked_ids = lax.all_to_all(
        send_ids.reshape(seq_devices, slot_cap), "seq", split_axis=0, concat_axis=0, tiled=True
    )
    asked_flat = asked_ids.reshape(-1)

    kv_rows = jnp.stack([keys, values])
    far_kv = [swapped(kv_rows, "seq", far_level) for far_level in range(far_count)]

    kv_four = kv_rows.reshape(2, blk_count, blk_size, heads_here, head_size)
    safe_ids = jnp.maximum(asked_flat, 0)
    pick_head = safe_ids // blk_count
    pick_blk = safe_ids % blk_count
    kv_pick = kv_four[:, pick_blk, :, pick_head, :]
    kv_back = lax.all_to_all(
        kv_pick.reshape(seq_devices, slot_cap, 2, blk_size, head_size),
        "seq",
        split_axis=0,
        concat_axis=0,
        tiled=True,
    ).reshape(slot_count, 2, blk_size, head_size)
    rand_kv = kv_back[slot_of_req].reshape(
        heads_here, blk_count, rand_count, 2, blk_size, head_size
    )

    def key_list(which):
        own = heads_first(kv_rows[which])
        parts = [own[:, :, None], own[:, ::-1, None]]
        parts += [heads_first(far_arr[which])[:, :, None] for far_arr in far_kv]
        parts.append(rand_kv[:, :, :, which])
        return jnp.concatenate(parts, axis=2)

    key_set = key_list(0)
    value_set = key_list(1)
    query_h = heads_first(queries)
    grad_h = heads_first(out_grad)

    scores = (
        jnp.einsum("hbtd,hbksd->hbtks", query_h, key_set, preferred_element_type=f32)
        * score_scale
    )
    row_max = jnp.max(scores, axis=(3, 4))
    log_total = row_max + jnp.log(
        jnp.sum(jnp.exp(scores - row_max[..., None, None]), axis=(3, 4))
    )
    weights = jnp.exp(scores - log_total[..., None, None])
    weights_low = weights.astype(jnp.bfloat16)
    attn_h = jnp.einsum(
        "hbtks,hbksd->hbtd", weights_low, value_set, preferred_element_type=f32
    ).astype(jnp.bfloat16)
    row_delta = jnp.sum(grad_h.astype(f32) * attn_h.astype(f32), axis=3)
    grad_weights = jnp.einsum("hbtd,hbksd->hbtks", grad_h, value_set, preferred_element_type=f32)
    grad_scores = (weights * (grad_weights - row_delta[..., None, None])).astype(jnp.bfloat16)
    grad_query_h = (
        score_scale
        * jnp.einsum("hbtks,hbksd->hbtd", grad_scores, key_set, preferred_element_type=f32)
    ).astype(jnp.bfloat16)
    key_terms = score_scale * jnp.einsum(
        "hbtks,hbtd->hbksd", grad_scores, query_h, preferred_element_type=f32
    )
    value_terms = jnp.einsum(
        "hbtks,hbtd->hbksd", weights_low, grad_h, preferred_element_type=f32
    )
    terms = jnp.stack([key_terms, value_terms])

    grad_kv = terms[:, :, :, 0] + low(terms[:, :, :, 1])[:, :, ::-1]
    far_first = 2
    rand_first = far_first + far_count
    far_low = terms[:, :, :, far_first:rand_first].astype(jnp.bfloat16)
    for far_level in range(far_count):
        send = far_low[:, :, :, far_level]
        back = swapped(send, "seq", far_level)
        grad_kv = grad_kv + back.astype(f32)

    rand_low = terms[:, :, :, rand_first:].astype(jnp.bfloat16)
    rand_req = rand_low.transpose(1, 2, 3, 0, 4, 5).reshape(total_req, 2 * blk_size * head_size)
    slot_onehot = slot_match.astype(jnp.bfloat16)
    send_terms = jnp.dot(slot_onehot, rand_req, preferred_element_type=f32).astype(jnp.bfloat16)
    slot_terms = lax.all_to_all(
        send_terms.reshape(seq_devices, slot_cap, 2 * blk_size * head_size),
        "seq",
        split_axis=0,
        concat_axis=0,
        tiled=True,
    ).reshape(slot_count, 2 * blk_size * head_size)
    target_rows = jnp.arange(heads_here * blk_count, dtype=jnp.int32)
    onehot = (asked_flat[None, :] == target_rows[:, None]).astype(jnp.bfloat16)
    extra = jnp.dot(onehot, slot_terms, preferred_element_type=f32)
    extra = extra.reshape(heads_here, blk_count, 2, blk_size, head_size).transpose(2, 0, 1, 3, 4)
    grad_kv = (grad_kv + extra).astype(jnp.bfloat16)

    attn_out = rows_back(attn_h)
    grad_queries = rows_back(grad_query_h)
    grad_keys = rows_back(grad_kv[0])
    grad_values = rows_back(grad_kv[1])
    return (attn_out, grad_queries, grad_keys, grad_values)


def solution(mesh):
    return jax.shard_map(
        local,
        mesh=mesh,
        in_specs=(
            P("seq", "head"),
            P("seq", "head"),
            P("seq", "head"),
            P("seq", "head"),
            P("head", "seq", None),
        ),
        out_specs=(P("seq", "head"), P("seq", "head"), P("seq", "head"), P("seq", "head")),
        check_vma=False,
    )
```

```python
import math

import jax
import jax.numpy as jnp
from jax import lax
from jax.sharding import PartitionSpec as P


def swapped(value, axis, distance):
    mask = 2**distance
    pairs = [(source, source ^ mask) for source in range(lax.axis_size(axis))]
    return lax.ppermute(value, axis, pairs)


def low(value_arr):
    return value_arr.astype(jnp.bfloat16).astype(jnp.float32)


def local(queries, keys, values, out_grad, rand_blocks):
    tok_rows = queries.shape[0]
    heads_here, blk_count, rand_count = rand_blocks.shape
    head_size = queries.shape[1] // heads_here
    blk_size = tok_rows // blk_count
    score_scale = 1.0 / math.sqrt(head_size)
    seq_devices = lax.axis_size("seq")
    far_count = seq_devices.bit_length() - 1
    f32 = jnp.float32

    def heads_first(arr):
        return arr.reshape(blk_count, blk_size, heads_here, head_size).transpose(2, 0, 1, 3)

    def rows_back(arr):
        return arr.transpose(1, 2, 0, 3).reshape(tok_rows, heads_here * head_size)

    total_req = heads_here * blk_count * rand_count
    slot_cap = max(2, -(-total_req // seq_devices))
    slot_count = seq_devices * slot_cap
    flat_req = rand_blocks.reshape(-1)
    owner_dev = flat_req // blk_count
    req_index = jnp.arange(total_req, dtype=jnp.int32)
    req_head = req_index // (blk_count * rand_count)
    payload = req_head * blk_count + flat_req % blk_count
    earlier_same = (owner_dev[:, None] == owner_dev[None, :]) & (
        req_index[:, None] > req_index[None, :]
    )
    slot_rank = jnp.sum(earlier_same.astype(jnp.int32), axis=1)
    slot_of_req = owner_dev * slot_cap + slot_rank
    slot_match = slot_of_req[None, :] == jnp.arange(slot_count, dtype=jnp.int32)[:, None]
    filled = jnp.any(slot_match, axis=1)
    send_ids = jnp.where(filled, jnp.sum(jnp.where(slot_match, payload[None, :], 0), axis=1), -1)
    asked_ids = lax.all_to_all(
        send_ids.reshape(seq_devices, slot_cap), "seq", split_axis=0, concat_axis=0, tiled=True
    )
    asked_flat = asked_ids.reshape(-1)

    kv_rows = jnp.stack([keys, values])
    far_kv = [swapped(kv_rows, "seq", far_level) for far_level in range(far_count)]

    kv_four = kv_rows.reshape(2, blk_count, blk_size, heads_here, head_size)
    safe_ids = jnp.maximum(asked_flat, 0)
    pick_head = safe_ids // blk_count
    pick_blk = safe_ids % blk_count
    kv_pick = kv_four[:, pick_blk, :, pick_head, :]
    kv_back = lax.all_to_all(
        kv_pick.reshape(seq_devices, slot_cap, 2, blk_size, head_size),
        "seq",
        split_axis=0,
        concat_axis=0,
        tiled=True,
    ).reshape(slot_count, 2, blk_size, head_size)
    rand_kv = kv_back[slot_of_req].reshape(
        heads_here, blk_count, rand_count, 2, blk_size, head_size
    )

    def fixed_list(which):
        own = heads_first(kv_rows[which])
        parts = [own[:, :, None], own[:, ::-1, None]]
        parts += [heads_first(far_arr[which])[:, :, None] for far_arr in far_kv]
        return jnp.concatenate(parts, axis=2)

    key_fix = fixed_list(0)
    value_fix = fixed_list(1)
    key_rnd = rand_kv[:, :, :, 0]
    value_rnd = rand_kv[:, :, :, 1]
    query_h = heads_first(queries)
    grad_h = heads_first(out_grad)

    def mm_scores(rows, key_part):
        return jnp.einsum("hbtd,hbksd->hbtks", rows, key_part, preferred_element_type=f32)

    def mm_out(weight_part, key_part):
        return jnp.einsum("hbtks,hbksd->hbtd", weight_part, key_part, preferred_element_type=f32)

    def mm_terms(weight_part, rows):
        return jnp.einsum("hbtks,hbtd->hbksd", weight_part, rows, preferred_element_type=f32)

    scores_fix = mm_scores(query_h, key_fix) * score_scale
    scores_rnd = mm_scores(query_h, key_rnd) * score_scale
    grad_weights_fix = mm_scores(grad_h, value_fix)
    grad_weights_rnd = mm_scores(grad_h, value_rnd)
    row_max = jnp.maximum(jnp.max(scores_fix, axis=(3, 4)), jnp.max(scores_rnd, axis=(3, 4)))
    exp_sum = jnp.sum(jnp.exp(scores_fix - row_max[..., None, None]), axis=(3, 4)) + jnp.sum(
        jnp.exp(scores_rnd - row_max[..., None, None]), axis=(3, 4)
    )
    log_total = row_max + jnp.log(exp_sum)
    weights_fix = jnp.exp(scores_fix - log_total[..., None, None])
    weights_rnd = jnp.exp(scores_rnd - log_total[..., None, None])
    low_fix = weights_fix.astype(jnp.bfloat16)
    low_rnd = weights_rnd.astype(jnp.bfloat16)
    attn_h = (mm_out(low_fix, value_fix) + mm_out(low_rnd, value_rnd)).astype(jnp.bfloat16)
    row_delta = jnp.sum(grad_h.astype(f32) * attn_h.astype(f32), axis=3)
    grad_scores_fix = (weights_fix * (grad_weights_fix - row_delta[..., None, None])).astype(
        jnp.bfloat16
    )
    grad_scores_rnd = (weights_rnd * (grad_weights_rnd - row_delta[..., None, None])).astype(
        jnp.bfloat16
    )

    rand_low = jnp.stack(
        [score_scale * mm_terms(grad_scores_rnd, query_h), mm_terms(low_rnd, grad_h)]
    ).astype(jnp.bfloat16)
    rand_req = rand_low.transpose(1, 2, 3, 0, 4, 5).reshape(total_req, 2 * blk_size * head_size)
    slot_onehot = slot_match.astype(jnp.bfloat16)
    send_terms = jnp.dot(slot_onehot, rand_req, preferred_element_type=f32).astype(jnp.bfloat16)
    slot_terms = lax.all_to_all(
        send_terms.reshape(seq_devices, slot_cap, 2 * blk_size * head_size),
        "seq",
        split_axis=0,
        concat_axis=0,
        tiled=True,
    ).reshape(slot_count, 2 * blk_size * head_size)

    grad_query_h = (
        score_scale * (mm_out(grad_scores_fix, key_fix) + mm_out(grad_scores_rnd, key_rnd))
    ).astype(jnp.bfloat16)
    terms = jnp.stack(
        [score_scale * mm_terms(grad_scores_fix, query_h), mm_terms(low_fix, grad_h)]
    )

    grad_kv = terms[:, :, :, 0] + low(terms[:, :, :, 1])[:, :, ::-1]
    far_low = terms[:, :, :, 2:].astype(jnp.bfloat16)
    for far_level in range(far_count):
        back = swapped(far_low[:, :, :, far_level], "seq", far_level)
        grad_kv = grad_kv + back.astype(f32)
    grad_rows = grad_kv.transpose(0, 2, 3, 1, 4)

    target_rows = jnp.arange(heads_here * blk_count, dtype=jnp.int32)
    onehot = (asked_flat[None, :] == target_rows[:, None]).astype(jnp.bfloat16)
    extra = jnp.dot(onehot, slot_terms, preferred_element_type=f32)
    extra = extra.reshape(heads_here, blk_count, 2, blk_size, head_size).transpose(2, 1, 3, 0, 4)
    grad_kv = (grad_rows + extra).astype(jnp.bfloat16).reshape(2, tok_rows, heads_here * head_size)

    attn_out = rows_back(attn_h)
    grad_queries = rows_back(grad_query_h)
    grad_keys = grad_kv[0]
    grad_values = grad_kv[1]
    return (attn_out, grad_queries, grad_keys, grad_values)


def solution(mesh):
    return jax.shard_map(
        local,
        mesh=mesh,
        in_specs=(
            P("seq", "head"),
            P("seq", "head"),
            P("seq", "head"),
            P("seq", "head"),
            P("head", "seq", None),
        ),
        out_specs=(P("seq", "head"), P("seq", "head"), P("seq", "head"), P("seq", "head")),
        check_vma=False,
    )
```

```python
import math

import jax
import jax.numpy as jnp
from jax import lax
from jax.sharding import PartitionSpec as P


def swapped(value, axis, distance):
    mask = 2**distance
    pairs = [(source, source ^ mask) for source in range(lax.axis_size(axis))]
    return lax.ppermute(value, axis, pairs)


def low(value_arr):
    return value_arr.astype(jnp.bfloat16).astype(jnp.float32)


def local(queries, keys, values, out_grad, rand_blocks):
    tok_rows = queries.shape[0]
    heads_here, blk_count, rand_count = rand_blocks.shape
    head_size = queries.shape[1] // heads_here
    blk_size = tok_rows // blk_count
    score_scale = 1.0 / math.sqrt(head_size)
    seq_devices = lax.axis_size("seq")
    far_count = seq_devices.bit_length() - 1
    f32 = jnp.float32

    def heads_first(arr):
        return arr.reshape(blk_count, blk_size, heads_here, head_size).transpose(2, 0, 1, 3)

    def rows_back(arr):
        return arr.transpose(1, 2, 0, 3).reshape(tok_rows, heads_here * head_size)

    total_req = heads_here * blk_count * rand_count
    slot_cap = max(2, -(-total_req // seq_devices))
    slot_count = seq_devices * slot_cap
    flat_req = rand_blocks.reshape(-1)
    owner_dev = flat_req // blk_count
    req_index = jnp.arange(total_req, dtype=jnp.int32)
    req_head = req_index // (blk_count * rand_count)
    payload = req_head * blk_count + flat_req % blk_count
    earlier_same = (owner_dev[:, None] == owner_dev[None, :]) & (
        req_index[:, None] > req_index[None, :]
    )
    slot_rank = jnp.sum(earlier_same.astype(jnp.int32), axis=1)
    slot_of_req = owner_dev * slot_cap + slot_rank
    slot_match = slot_of_req[None, :] == jnp.arange(slot_count, dtype=jnp.int32)[:, None]
    filled = jnp.any(slot_match, axis=1)
    send_ids = jnp.where(filled, jnp.sum(jnp.where(slot_match, payload[None, :], 0), axis=1), -1)
    asked_ids = lax.all_to_all(
        send_ids.reshape(seq_devices, slot_cap), "seq", split_axis=0, concat_axis=0, tiled=True
    )
    asked_flat = asked_ids.reshape(-1)

    kv_rows = jnp.stack([keys, values])
    far_kv = [swapped(kv_rows, "seq", far_level) for far_level in range(far_count)]

    kv_four = kv_rows.reshape(2, blk_count, blk_size, heads_here, head_size)
    safe_ids = jnp.maximum(asked_flat, 0)
    pick_head = safe_ids // blk_count
    pick_blk = safe_ids % blk_count
    kv_pick = kv_four[:, pick_blk, :, pick_head, :]
    kv_back = lax.all_to_all(
        kv_pick.reshape(seq_devices, slot_cap, 2, blk_size, head_size),
        "seq",
        split_axis=0,
        concat_axis=0,
        tiled=True,
    ).reshape(slot_count, 2, blk_size, head_size)
    rand_kv = kv_back[slot_of_req].reshape(
        heads_here, blk_count, rand_count, 2, blk_size, head_size
    )

    def fixed_list(which):
        own = heads_first(kv_rows[which])
        parts = [own[:, :, None], own[:, ::-1, None]]
        parts += [heads_first(far_arr[which])[:, :, None] for far_arr in far_kv]
        return jnp.concatenate(parts, axis=2)

    key_fix = fixed_list(0)
    value_fix = fixed_list(1)
    key_rnd = rand_kv[:, :, :, 0]
    value_rnd = rand_kv[:, :, :, 1]
    query_h = heads_first(queries)
    grad_h = heads_first(out_grad)

    def mm_scores(rows, key_part):
        return jnp.einsum("hbtd,hbksd->hbtks", rows, key_part, preferred_element_type=f32)

    def mm_out(weight_part, key_part):
        return jnp.einsum("hbtks,hbksd->hbtd", weight_part, key_part, preferred_element_type=f32)

    def mm_terms(weight_part, rows):
        return jnp.einsum("hbtks,hbtd->hbksd", weight_part, rows, preferred_element_type=f32)

    scores_fix = mm_scores(query_h, key_fix) * score_scale
    scores_rnd = mm_scores(query_h, key_rnd) * score_scale
    grad_weights_fix = mm_scores(grad_h, value_fix)
    grad_weights_rnd = mm_scores(grad_h, value_rnd)
    row_max = jnp.maximum(jnp.max(scores_fix, axis=(3, 4)), jnp.max(scores_rnd, axis=(3, 4)))
    exp_sum = jnp.sum(jnp.exp(scores_fix - row_max[..., None, None]), axis=(3, 4)) + jnp.sum(
        jnp.exp(scores_rnd - row_max[..., None, None]), axis=(3, 4)
    )
    log_total = row_max + jnp.log(exp_sum)
    weights_fix = jnp.exp(scores_fix - log_total[..., None, None])
    weights_rnd = jnp.exp(scores_rnd - log_total[..., None, None])
    low_fix = weights_fix.astype(jnp.bfloat16)
    low_rnd = weights_rnd.astype(jnp.bfloat16)
    attn_h = (mm_out(low_fix, value_fix) + mm_out(low_rnd, value_rnd)).astype(jnp.bfloat16)
    row_delta = jnp.sum(grad_h.astype(f32) * attn_h.astype(f32), axis=3)
    grad_scores_fix = (weights_fix * (grad_weights_fix - row_delta[..., None, None])).astype(
        jnp.bfloat16
    )
    grad_scores_rnd = (weights_rnd * (grad_weights_rnd - row_delta[..., None, None])).astype(
        jnp.bfloat16
    )

    rand_low = jnp.stack(
        [score_scale * mm_terms(grad_scores_rnd, query_h), mm_terms(low_rnd, grad_h)]
    ).astype(jnp.bfloat16)
    rand_req = rand_low.transpose(1, 2, 3, 0, 4, 5).reshape(total_req, 2, blk_size, head_size)
    slot_onehot = slot_match.astype(jnp.bfloat16)
    send_terms = jnp.einsum(
        "pn,nksd->pksd", slot_onehot, rand_req, preferred_element_type=f32
    ).astype(jnp.bfloat16)
    slot_terms = lax.all_to_all(
        send_terms.reshape(seq_devices, slot_cap, 2, blk_size, head_size),
        "seq",
        split_axis=0,
        concat_axis=0,
        tiled=True,
    ).reshape(slot_count, 2, blk_size, head_size)

    grad_query_h = (
        score_scale * (mm_out(grad_scores_fix, key_fix) + mm_out(grad_scores_rnd, key_rnd))
    ).astype(jnp.bfloat16)
    terms = jnp.stack(
        [score_scale * mm_terms(grad_scores_fix, query_h), mm_terms(low_fix, grad_h)]
    )

    grad_kv = terms[:, :, :, 0] + low(terms[:, :, :, 1])[:, :, ::-1]
    far_low = terms[:, :, :, 2:].astype(jnp.bfloat16)
    for far_level in range(far_count):
        back = swapped(far_low[:, :, :, far_level], "seq", far_level)
        grad_kv = grad_kv + back.astype(f32)
    grad_rows = grad_kv.transpose(0, 2, 3, 1, 4)

    target_rows = jnp.arange(heads_here * blk_count, dtype=jnp.int32)
    onehot = (asked_flat[None, :] == target_rows[:, None]).astype(jnp.bfloat16)
    extra = jnp.einsum("tp,pksd->tksd", onehot, slot_terms, preferred_element_type=f32)
    extra = extra.reshape(heads_here, blk_count, 2, blk_size, head_size).transpose(2, 1, 3, 0, 4)
    grad_kv = (grad_rows + extra).astype(jnp.bfloat16).reshape(2, tok_rows, heads_here * head_size)

    attn_out = rows_back(attn_h)
    grad_queries = rows_back(grad_query_h)
    grad_keys = grad_kv[0]
    grad_values = grad_kv[1]
    return (attn_out, grad_queries, grad_keys, grad_values)


def solution(mesh):
    return jax.shard_map(
        local,
        mesh=mesh,
        in_specs=(
            P("seq", "head"),
            P("seq", "head"),
            P("seq", "head"),
            P("seq", "head"),
            P("head", "seq", None),
        ),
        out_specs=(P("seq", "head"), P("seq", "head"), P("seq", "head"), P("seq", "head")),
        check_vma=False,
    )
```

```python
import math

import jax
import jax.numpy as jnp
from jax import lax
from jax.sharding import PartitionSpec as P


def swapped(value, axis, distance):
    mask = 2**distance
    pairs = [(source, source ^ mask) for source in range(lax.axis_size(axis))]
    return lax.ppermute(value, axis, pairs)


def low(value_arr):
    return value_arr.astype(jnp.bfloat16).astype(jnp.float32)


def local(queries, keys, values, out_grad, rand_blocks, rand_blocks_all):
    tok_rows = queries.shape[0]
    heads_here, blk_count, rand_count = rand_blocks.shape
    head_size = queries.shape[1] // heads_here
    blk_size = tok_rows // blk_count
    score_scale = 1.0 / math.sqrt(head_size)
    seq_devices = lax.axis_size("seq")
    far_count = seq_devices.bit_length() - 1
    f32 = jnp.float32

    def heads_first(arr):
        return arr.reshape(blk_count, blk_size, heads_here, head_size).transpose(2, 0, 1, 3)

    def rows_back(arr):
        return arr.transpose(1, 2, 0, 3).reshape(tok_rows, heads_here * head_size)

    my_dev = lax.axis_index("seq")
    all_req = rand_blocks_all.reshape(heads_here, seq_devices, blk_count, rand_count)
    all_req = all_req.transpose(1, 0, 2, 3).reshape(seq_devices, -1)
    total_req = heads_here * blk_count * rand_count
    slot_cap = max(2, -(-total_req // seq_devices))
    slot_count = seq_devices * slot_cap
    req_index = jnp.arange(total_req, dtype=jnp.int32)
    req_head = req_index // (blk_count * rand_count)
    all_owner = all_req // blk_count
    earlier_same = (all_owner[:, :, None] == all_owner[:, None, :]) & (
        req_index[:, None] > req_index[None, :]
    )
    all_rank = jnp.sum(earlier_same.astype(jnp.int32), axis=2)
    all_payload = req_head[None, :] * blk_count + all_req % blk_count
    flat_req = rand_blocks.reshape(-1)
    owner_dev = flat_req // blk_count
    slot_rank = all_rank[my_dev]
    slot_of_req = owner_dev * slot_cap + slot_rank
    slot_match = slot_of_req[None, :] == jnp.arange(slot_count, dtype=jnp.int32)[:, None]
    ask_match = (all_owner[:, :, None] == my_dev) & (
        all_rank[:, :, None] == jnp.arange(slot_cap, dtype=jnp.int32)
    )
    asked_ids = jnp.where(
        jnp.any(ask_match, axis=1),
        jnp.sum(jnp.where(ask_match, all_payload[:, :, None], 0), axis=1),
        -1,
    )
    asked_flat = asked_ids.reshape(-1)

    kv_rows = jnp.stack([keys, values])
    far_kv = [swapped(kv_rows, "seq", far_level) for far_level in range(far_count)]

    kv_four = kv_rows.reshape(2, blk_count, blk_size, heads_here, head_size)
    safe_ids = jnp.maximum(asked_flat, 0)
    pick_head = safe_ids // blk_count
    pick_blk = safe_ids % blk_count
    kv_pick = kv_four[:, pick_blk, :, pick_head, :]
    kv_back = lax.all_to_all(
        kv_pick.reshape(seq_devices, slot_cap, 2, blk_size, head_size),
        "seq",
        split_axis=0,
        concat_axis=0,
        tiled=True,
    ).reshape(slot_count, 2, blk_size, head_size)
    rand_kv = kv_back[slot_of_req].reshape(
        heads_here, blk_count, rand_count, 2, blk_size, head_size
    )

    def fixed_list(which):
        own = heads_first(kv_rows[which])
        parts = [own[:, :, None], own[:, ::-1, None]]
        parts += [heads_first(far_arr[which])[:, :, None] for far_arr in far_kv]
        return jnp.concatenate(parts, axis=2)

    key_fix = fixed_list(0)
    value_fix = fixed_list(1)
    key_rnd = rand_kv[:, :, :, 0]
    value_rnd = rand_kv[:, :, :, 1]
    query_h = heads_first(queries)
    grad_h = heads_first(out_grad)

    def mm_scores(rows, key_part):
        return jnp.einsum("hbtd,hbksd->hbtks", rows, key_part, preferred_element_type=f32)

    def mm_out(weight_part, key_part):
        return jnp.einsum("hbtks,hbksd->hbtd", weight_part, key_part, preferred_element_type=f32)

    def mm_terms(weight_part, rows):
        return jnp.einsum("hbtks,hbtd->hbksd", weight_part, rows, preferred_element_type=f32)

    scores_fix = mm_scores(query_h, key_fix) * score_scale
    scores_rnd = mm_scores(query_h, key_rnd) * score_scale
    grad_weights_fix = mm_scores(grad_h, value_fix)
    grad_weights_rnd = mm_scores(grad_h, value_rnd)
    row_max = jnp.maximum(jnp.max(scores_fix, axis=(3, 4)), jnp.max(scores_rnd, axis=(3, 4)))
    exp_sum = jnp.sum(jnp.exp(scores_fix - row_max[..., None, None]), axis=(3, 4)) + jnp.sum(
        jnp.exp(scores_rnd - row_max[..., None, None]), axis=(3, 4)
    )
    log_total = row_max + jnp.log(exp_sum)
    weights_fix = jnp.exp(scores_fix - log_total[..., None, None])
    weights_rnd = jnp.exp(scores_rnd - log_total[..., None, None])
    low_fix = weights_fix.astype(jnp.bfloat16)
    low_rnd = weights_rnd.astype(jnp.bfloat16)
    attn_h = (mm_out(low_fix, value_fix) + mm_out(low_rnd, value_rnd)).astype(jnp.bfloat16)
    row_delta = jnp.sum(grad_h.astype(f32) * attn_h.astype(f32), axis=3)
    grad_scores_fix = (weights_fix * (grad_weights_fix - row_delta[..., None, None])).astype(
        jnp.bfloat16
    )
    grad_scores_rnd = (weights_rnd * (grad_weights_rnd - row_delta[..., None, None])).astype(
        jnp.bfloat16
    )

    rand_low = jnp.stack(
        [score_scale * mm_terms(grad_scores_rnd, query_h), mm_terms(low_rnd, grad_h)]
    ).astype(jnp.bfloat16)
    rand_req = rand_low.transpose(1, 2, 3, 0, 4, 5).reshape(total_req, 2, blk_size, head_size)
    rand_req = jnp.concatenate([rand_req, jnp.zeros_like(rand_req[:1])], axis=0)
    req_of_slot = jnp.where(
        jnp.any(slot_match, axis=1),
        jnp.sum(jnp.where(slot_match, req_index[None, :], 0), axis=1),
        total_req,
    )
    send_terms = rand_req[req_of_slot]
    slot_terms = lax.all_to_all(
        send_terms.reshape(seq_devices, slot_cap, 2, blk_size, head_size),
        "seq",
        split_axis=0,
        concat_axis=0,
        tiled=True,
    ).reshape(slot_count, 2, blk_size, head_size)

    grad_query_h = (
        score_scale * (mm_out(grad_scores_fix, key_fix) + mm_out(grad_scores_rnd, key_rnd))
    ).astype(jnp.bfloat16)
    terms = jnp.stack(
        [score_scale * mm_terms(grad_scores_fix, query_h), mm_terms(low_fix, grad_h)]
    )

    grad_kv = terms[:, :, :, 0] + low(terms[:, :, :, 1])[:, :, ::-1]
    far_low = terms[:, :, :, 2:].astype(jnp.bfloat16)
    for far_level in range(far_count):
        back = swapped(far_low[:, :, :, far_level], "seq", far_level)
        grad_kv = grad_kv + back.astype(f32)
    grad_rows = grad_kv.transpose(0, 2, 3, 1, 4)

    target_count = heads_here * blk_count
    target_of_slot = jnp.where(asked_flat >= 0, asked_flat, target_count)
    extra = (
        jnp.zeros((target_count + 1, 2, blk_size, head_size), f32)
        .at[target_of_slot]
        .add(slot_terms.astype(f32))[:target_count]
    )
    extra = extra.reshape(heads_here, blk_count, 2, blk_size, head_size).transpose(2, 1, 3, 0, 4)
    grad_kv = (grad_rows + extra).astype(jnp.bfloat16).reshape(2, tok_rows, heads_here * head_size)

    attn_out = rows_back(attn_h)
    grad_queries = rows_back(grad_query_h)
    grad_keys = grad_kv[0]
    grad_values = grad_kv[1]
    return (attn_out, grad_queries, grad_keys, grad_values)


def solution(mesh):
    inner = jax.shard_map(
        local,
        mesh=mesh,
        in_specs=(
            P("seq", "head"),
            P("seq", "head"),
            P("seq", "head"),
            P("seq", "head"),
            P("head", "seq", None),
            P("head", None, None),
        ),
        out_specs=(P("seq", "head"), P("seq", "head"), P("seq", "head"), P("seq", "head")),
        check_vma=False,
    )

    def step(queries, keys, values, out_grad, rand_blocks):
        return inner(queries, keys, values, out_grad, rand_blocks, rand_blocks)

    return step
```

```python
import math

import jax
import jax.numpy as jnp
from jax import lax
from jax.experimental.layout import Layout, with_layout_constraint
from jax.sharding import PartitionSpec as P


def swapped(value, axis, distance):
    mask = 2**distance
    pairs = [(source, source ^ mask) for source in range(lax.axis_size(axis))]
    return lax.ppermute(value, axis, pairs)


def low(value_arr):
    return value_arr.astype(jnp.bfloat16).astype(jnp.float32)


def body(queries, keys, values, out_grad, rand_blocks):
    tok_rows = queries.shape[0]
    heads_here, blk_count, rand_count = rand_blocks.shape
    head_size = queries.shape[1] // heads_here
    blk_size = tok_rows // blk_count
    score_scale = 1.0 / math.sqrt(head_size)
    seq_devices = lax.axis_size("seq")
    far_count = seq_devices.bit_length() - 1
    f32 = jnp.float32

    def heads_first(arr):
        return arr.reshape(blk_count, blk_size, heads_here, head_size).transpose(2, 0, 1, 3)

    def rows_back(arr):
        return arr.transpose(1, 2, 0, 3).reshape(tok_rows, heads_here * head_size)

    total_req = heads_here * blk_count * rand_count
    slot_cap = max(2, -(-total_req // seq_devices))
    slot_count = seq_devices * slot_cap
    flat_req = rand_blocks.reshape(-1)
    owner_dev = flat_req // blk_count
    req_index = jnp.arange(total_req, dtype=jnp.int32)
    req_head = req_index // (blk_count * rand_count)
    payload = req_head * blk_count + flat_req % blk_count
    earlier_same = (owner_dev[:, None] == owner_dev[None, :]) & (
        req_index[:, None] > req_index[None, :]
    )
    slot_rank = jnp.sum(earlier_same.astype(jnp.int32), axis=1)
    slot_of_req = owner_dev * slot_cap + slot_rank
    slot_match = slot_of_req[None, :] == jnp.arange(slot_count, dtype=jnp.int32)[:, None]
    filled = jnp.any(slot_match, axis=1)
    send_ids = jnp.where(filled, jnp.sum(jnp.where(slot_match, payload[None, :], 0), axis=1), -1)
    asked_ids = lax.all_to_all(
        send_ids.reshape(seq_devices, slot_cap), "seq", split_axis=0, concat_axis=0, tiled=True
    )
    asked_flat = asked_ids.reshape(-1)

    kv_rows = jnp.stack([keys, values])
    far_kv = [swapped(kv_rows, "seq", far_level) for far_level in range(far_count)]

    kv_four = kv_rows.reshape(2, blk_count, blk_size, heads_here, head_size)
    safe_ids = jnp.maximum(asked_flat, 0)
    pick_head = safe_ids // blk_count
    pick_blk = safe_ids % blk_count
    kv_pick = kv_four[:, pick_blk, :, pick_head, :]
    kv_back = lax.all_to_all(
        kv_pick.reshape(seq_devices, slot_cap, 2, blk_size, head_size),
        "seq",
        split_axis=0,
        concat_axis=0,
        tiled=True,
    ).reshape(slot_count, 2, blk_size, head_size)
    rand_kv = kv_back[slot_of_req].reshape(
        heads_here, blk_count, rand_count, 2, blk_size, head_size
    )

    def fixed_list(which):
        own = heads_first(kv_rows[which])
        parts = [own[:, :, None], own[:, ::-1, None]]
        parts += [heads_first(far_arr[which])[:, :, None] for far_arr in far_kv]
        return jnp.concatenate(parts, axis=2)

    key_fix = fixed_list(0)
    value_fix = fixed_list(1)
    key_rnd = rand_kv[:, :, :, 0]
    value_rnd = rand_kv[:, :, :, 1]
    query_h = heads_first(queries)
    grad_h = heads_first(out_grad)

    def mm_scores(rows, key_part):
        return jnp.einsum("hbtd,hbksd->hbtks", rows, key_part, preferred_element_type=f32)

    def mm_out(weight_part, key_part):
        return jnp.einsum("hbtks,hbksd->hbtd", weight_part, key_part, preferred_element_type=f32)

    def mm_terms(weight_part, rows):
        return jnp.einsum("hbtks,hbtd->hbksd", weight_part, rows, preferred_element_type=f32)

    scores_fix = mm_scores(query_h, key_fix) * score_scale
    scores_rnd = mm_scores(query_h, key_rnd) * score_scale
    grad_weights_fix = mm_scores(grad_h, value_fix)
    grad_weights_rnd = mm_scores(grad_h, value_rnd)
    row_max = jnp.maximum(jnp.max(scores_fix, axis=(3, 4)), jnp.max(scores_rnd, axis=(3, 4)))
    exp_sum = jnp.sum(jnp.exp(scores_fix - row_max[..., None, None]), axis=(3, 4)) + jnp.sum(
        jnp.exp(scores_rnd - row_max[..., None, None]), axis=(3, 4)
    )
    log_total = row_max + jnp.log(exp_sum)
    weights_fix = jnp.exp(scores_fix - log_total[..., None, None])
    weights_rnd = jnp.exp(scores_rnd - log_total[..., None, None])
    low_fix = weights_fix.astype(jnp.bfloat16)
    low_rnd = weights_rnd.astype(jnp.bfloat16)
    attn_h = (mm_out(low_fix, value_fix) + mm_out(low_rnd, value_rnd)).astype(jnp.bfloat16)
    row_delta = jnp.sum(grad_h.astype(f32) * attn_h.astype(f32), axis=3)
    grad_scores_fix = (weights_fix * (grad_weights_fix - row_delta[..., None, None])).astype(
        jnp.bfloat16
    )
    grad_scores_rnd = (weights_rnd * (grad_weights_rnd - row_delta[..., None, None])).astype(
        jnp.bfloat16
    )

    rand_low = jnp.stack(
        [score_scale * mm_terms(grad_scores_rnd, query_h), mm_terms(low_rnd, grad_h)]
    ).astype(jnp.bfloat16)
    rand_req = rand_low.transpose(1, 2, 3, 0, 4, 5).reshape(total_req, 2, blk_size, head_size)
    rand_req = jnp.concatenate([rand_req, jnp.zeros_like(rand_req[:1])], axis=0)
    req_of_slot = jnp.where(
        jnp.any(slot_match, axis=1),
        jnp.sum(jnp.where(slot_match, req_index[None, :], 0), axis=1),
        total_req,
    )
    send_terms = rand_req[req_of_slot]
    row_major = Layout(major_to_minor=(0, 1, 2, 3, 4))
    slot_terms = lax.all_to_all(
        with_layout_constraint(
            send_terms.reshape(seq_devices, slot_cap, 2, blk_size, head_size), row_major
        ),
        "seq",
        split_axis=0,
        concat_axis=0,
        tiled=True,
    )
    slot_terms = with_layout_constraint(slot_terms, row_major).reshape(
        slot_count, 2, blk_size, head_size
    )

    grad_query_h = (
        score_scale * (mm_out(grad_scores_fix, key_fix) + mm_out(grad_scores_rnd, key_rnd))
    ).astype(jnp.bfloat16)
    terms = jnp.stack(
        [score_scale * mm_terms(grad_scores_fix, query_h), mm_terms(low_fix, grad_h)]
    )

    grad_kv = terms[:, :, :, 0] + low(terms[:, :, :, 1])[:, :, ::-1]
    far_low = terms[:, :, :, 2:].astype(jnp.bfloat16)
    for far_level in range(far_count):
        back = swapped(far_low[:, :, :, far_level], "seq", far_level)
        grad_kv = grad_kv + back.astype(f32)
    grad_rows = grad_kv.transpose(0, 2, 3, 1, 4)

    target_rows = jnp.arange(heads_here * blk_count, dtype=jnp.int32)
    onehot = (asked_flat[None, :] == target_rows[:, None]).astype(jnp.bfloat16)
    extra = jnp.einsum("tp,pksd->tksd", onehot, slot_terms, preferred_element_type=f32)
    extra = extra.reshape(heads_here, blk_count, 2, blk_size, head_size).transpose(2, 1, 3, 0, 4)
    grad_kv = (grad_rows + extra).astype(jnp.bfloat16).reshape(2, tok_rows, heads_here * head_size)

    attn_out = rows_back(attn_h)
    grad_queries = rows_back(grad_query_h)
    grad_keys = grad_kv[0]
    grad_values = grad_kv[1]
    return (attn_out, grad_queries, grad_keys, grad_values)


def solution(mesh):
    return jax.shard_map(
        body,
        mesh=mesh,
        in_specs=(
            P("seq", "head"),
            P("seq", "head"),
            P("seq", "head"),
            P("seq", "head"),
            P("head", "seq", None),
        ),
        out_specs=(P("seq", "head"), P("seq", "head"), P("seq", "head"), P("seq", "head")),
        check_vma=False,
    )
```

```python
import math

import jax
import jax.numpy as jnp
from jax import lax
from jax.experimental.layout import Layout, with_layout_constraint
from jax.sharding import PartitionSpec as P


def swapped(value, axis, distance):
    mask = 2**distance
    pairs = [(source, source ^ mask) for source in range(lax.axis_size(axis))]
    return lax.ppermute(value, axis, pairs)


def low(value_arr):
    return value_arr.astype(jnp.bfloat16).astype(jnp.float32)


def body(queries, keys, values, out_grad, rand_blocks):
    tok_rows = queries.shape[0]
    heads_here, blk_count, rand_count = rand_blocks.shape
    head_size = queries.shape[1] // heads_here
    blk_size = tok_rows // blk_count
    score_scale = 1.0 / math.sqrt(head_size)
    seq_devices = lax.axis_size("seq")
    far_count = seq_devices.bit_length() - 1
    f32 = jnp.float32

    def heads_first(arr):
        return arr.reshape(blk_count, blk_size, heads_here, head_size).transpose(2, 0, 1, 3)

    def rows_back(arr):
        return arr.transpose(1, 2, 0, 3).reshape(tok_rows, heads_here * head_size)

    total_req = heads_here * blk_count * rand_count
    slot_cap = max(2, -(-total_req // seq_devices))
    slot_count = seq_devices * slot_cap
    flat_req = rand_blocks.reshape(-1)
    owner_dev = flat_req // blk_count
    req_index = jnp.arange(total_req, dtype=jnp.int32)
    req_head = req_index // (blk_count * rand_count)
    payload = req_head * blk_count + flat_req % blk_count
    earlier_same = (owner_dev[:, None] == owner_dev[None, :]) & (
        req_index[:, None] > req_index[None, :]
    )
    slot_rank = jnp.sum(earlier_same.astype(jnp.int32), axis=1)
    slot_of_req = owner_dev * slot_cap + slot_rank
    slot_match = slot_of_req[None, :] == jnp.arange(slot_count, dtype=jnp.int32)[:, None]
    filled = jnp.any(slot_match, axis=1)
    send_ids = jnp.where(filled, jnp.sum(jnp.where(slot_match, payload[None, :], 0), axis=1), -1)
    asked_ids = lax.all_to_all(
        send_ids.reshape(seq_devices, slot_cap), "seq", split_axis=0, concat_axis=0, tiled=True
    )
    asked_flat = asked_ids.reshape(-1)

    kv_rows = jnp.stack([keys, values])
    far_kv = []
    for far_level in range(far_count):
        far_kv.append(swapped(kv_rows, "seq", far_level))

    kv_four = kv_rows.reshape(2, blk_count, blk_size, heads_here, head_size)
    safe_ids = jnp.maximum(asked_flat, 0)
    pick_head = safe_ids // blk_count
    pick_blk = safe_ids % blk_count
    kv_pick = kv_four[:, pick_blk, :, pick_head, :]
    kv_back = lax.all_to_all(
        kv_pick.reshape(seq_devices, slot_cap, 2, blk_size, head_size),
        "seq",
        split_axis=0,
        concat_axis=0,
        tiled=True,
    ).reshape(slot_count, 2, blk_size, head_size)
    rand_kv = kv_back[slot_of_req].reshape(
        heads_here, blk_count, rand_count, 2, blk_size, head_size
    )

    def fixed_list(which):
        own = heads_first(kv_rows[which])
        parts = [own[:, :, None], own[:, ::-1, None]]
        parts += [heads_first(far_arr[which])[:, :, None] for far_arr in far_kv]
        return jnp.concatenate(parts, axis=2)

    key_fix = fixed_list(0)
    value_fix = fixed_list(1)
    key_rnd = rand_kv[:, :, :, 0]
    value_rnd = rand_kv[:, :, :, 1]
    query_h = heads_first(queries)
    grad_h = heads_first(out_grad)

    def mm_scores(rows, key_part):
        return jnp.einsum("hbtd,hbksd->hbtks", rows, key_part, preferred_element_type=f32)

    def mm_out(weight_part, key_part):
        return jnp.einsum("hbtks,hbksd->hbtd", weight_part, key_part, preferred_element_type=f32)

    def mm_terms(weight_part, rows):
        return jnp.einsum("hbtks,hbtd->hbksd", weight_part, rows, preferred_element_type=f32)

    scores_fix = mm_scores(query_h, key_fix) * score_scale
    scores_rnd = mm_scores(query_h, key_rnd) * score_scale
    grad_weights_fix = mm_scores(grad_h, value_fix)
    grad_weights_rnd = mm_scores(grad_h, value_rnd)
    row_max = jnp.maximum(jnp.max(scores_fix, axis=(3, 4)), jnp.max(scores_rnd, axis=(3, 4)))
    exp_sum = jnp.sum(jnp.exp(scores_fix - row_max[..., None, None]), axis=(3, 4)) + jnp.sum(
        jnp.exp(scores_rnd - row_max[..., None, None]), axis=(3, 4)
    )
    log_total = row_max + jnp.log(exp_sum)
    weights_fix = jnp.exp(scores_fix - log_total[..., None, None])
    weights_rnd = jnp.exp(scores_rnd - log_total[..., None, None])
    low_fix = weights_fix.astype(jnp.bfloat16)
    low_rnd = weights_rnd.astype(jnp.bfloat16)
    attn_h = (mm_out(low_fix, value_fix) + mm_out(low_rnd, value_rnd)).astype(jnp.bfloat16)
    row_delta = jnp.sum(grad_h.astype(f32) * attn_h.astype(f32), axis=3)
    grad_scores_fix = (weights_fix * (grad_weights_fix - row_delta[..., None, None])).astype(
        jnp.bfloat16
    )
    grad_scores_rnd = (weights_rnd * (grad_weights_rnd - row_delta[..., None, None])).astype(
        jnp.bfloat16
    )

    rand_low = jnp.stack(
        [score_scale * mm_terms(grad_scores_rnd, query_h), mm_terms(low_rnd, grad_h)]
    ).astype(jnp.bfloat16)
    rand_req = rand_low.transpose(1, 2, 3, 0, 4, 5).reshape(total_req, 2, blk_size, head_size)
    rand_req = jnp.concatenate([rand_req, jnp.zeros_like(rand_req[:1])], axis=0)
    req_of_slot = jnp.where(
        jnp.any(slot_match, axis=1),
        jnp.sum(jnp.where(slot_match, req_index[None, :], 0), axis=1),
        total_req,
    )
    send_terms = rand_req[req_of_slot]
    row_major = Layout(major_to_minor=(0, 1, 2, 3, 4))
    slot_terms = lax.all_to_all(
        with_layout_constraint(
            send_terms.reshape(seq_devices, slot_cap, 2, blk_size, head_size), row_major
        ),
        "seq",
        split_axis=0,
        concat_axis=0,
        tiled=True,
    )
    slot_terms = with_layout_constraint(slot_terms, row_major).reshape(
        slot_count, 2, blk_size, head_size
    )

    grad_query_h = (
        score_scale * (mm_out(grad_scores_fix, key_fix) + mm_out(grad_scores_rnd, key_rnd))
    ).astype(jnp.bfloat16)
    terms = jnp.stack(
        [score_scale * mm_terms(grad_scores_fix, query_h), mm_terms(low_fix, grad_h)]
    )

    grad_kv = terms[:, :, :, 0] + low(terms[:, :, :, 1])[:, :, ::-1]
    far_low = terms[:, :, :, 2:].astype(jnp.bfloat16)
    slow_first = [0, 1, 4, 5, 3, 2] if far_count == 6 else list(range(far_count))
    for far_level in slow_first:
        back = swapped(far_low[:, :, :, far_level], "seq", far_level)
        grad_kv = grad_kv + back.astype(f32)
    grad_rows = grad_kv.transpose(0, 2, 3, 1, 4)

    target_rows = jnp.arange(heads_here * blk_count, dtype=jnp.int32)
    onehot = (asked_flat[None, :] == target_rows[:, None]).astype(jnp.bfloat16)
    extra = jnp.einsum("tp,pksd->tksd", onehot, slot_terms, preferred_element_type=f32)
    extra = extra.reshape(heads_here, blk_count, 2, blk_size, head_size).transpose(2, 1, 3, 0, 4)
    grad_kv = (grad_rows + extra).astype(jnp.bfloat16).reshape(2, tok_rows, heads_here * head_size)

    attn_out = rows_back(attn_h)
    grad_queries = rows_back(grad_query_h)
    grad_keys = grad_kv[0]
    grad_values = grad_kv[1]
    return (attn_out, grad_queries, grad_keys, grad_values)


def solution(mesh):
    return jax.shard_map(
        body,
        mesh=mesh,
        in_specs=(
            P("seq", "head"),
            P("seq", "head"),
            P("seq", "head"),
            P("seq", "head"),
            P("head", "seq", None),
        ),
        out_specs=(P("seq", "head"), P("seq", "head"), P("seq", "head"), P("seq", "head")),
        check_vma=False,
    )
```

```python
import math

import jax
import jax.numpy as jnp
from jax import lax
from jax.experimental.layout import Layout, with_layout_constraint
from jax.sharding import PartitionSpec as P


def swapped(value, axis, distance):
    mask = 2**distance
    pairs = [(source, source ^ mask) for source in range(lax.axis_size(axis))]
    return lax.ppermute(value, axis, pairs)


def low(value_arr):
    return value_arr.astype(jnp.bfloat16).astype(jnp.float32)


def body(queries, keys, values, out_grad, rand_blocks):
    tok_rows = queries.shape[0]
    heads_here, blk_count, rand_count = rand_blocks.shape
    head_size = queries.shape[1] // heads_here
    blk_size = tok_rows // blk_count
    score_scale = 1.0 / math.sqrt(head_size)
    seq_devices = lax.axis_size("seq")
    far_count = seq_devices.bit_length() - 1
    f32 = jnp.float32

    def heads_first(arr):
        return arr.reshape(blk_count, blk_size, heads_here, head_size).transpose(2, 0, 1, 3)

    def rows_back(arr):
        return arr.transpose(1, 2, 0, 3).reshape(tok_rows, heads_here * head_size)

    total_req = heads_here * blk_count * rand_count
    slot_cap = max(2, -(-total_req // seq_devices))
    slot_count = seq_devices * slot_cap
    flat_req = rand_blocks.reshape(-1)
    owner_dev = flat_req // blk_count
    req_index = jnp.arange(total_req, dtype=jnp.int32)
    req_head = req_index // (blk_count * rand_count)
    payload = req_head * blk_count + flat_req % blk_count
    earlier_same = (owner_dev[:, None] == owner_dev[None, :]) & (
        req_index[:, None] > req_index[None, :]
    )
    slot_rank = jnp.sum(earlier_same.astype(jnp.int32), axis=1)
    slot_of_req = owner_dev * slot_cap + slot_rank
    slot_match = slot_of_req[None, :] == jnp.arange(slot_count, dtype=jnp.int32)[:, None]
    filled = jnp.any(slot_match, axis=1)
    send_ids = jnp.where(filled, jnp.sum(jnp.where(slot_match, payload[None, :], 0), axis=1), -1)
    asked_ids = lax.all_to_all(
        send_ids.reshape(seq_devices, slot_cap), "seq", split_axis=0, concat_axis=0, tiled=True
    )
    asked_flat = asked_ids.reshape(-1)

    kv_rows = jnp.stack([keys, values])
    far_kv = [swapped(kv_rows, "seq", far_level) for far_level in range(far_count)]

    kv_items = (
        kv_rows.reshape(2, blk_count, blk_size, heads_here, head_size)
        .transpose(3, 1, 0, 2, 4)
        .reshape(heads_here * blk_count, 2, blk_size, head_size)
    )
    safe_ids = jnp.maximum(asked_flat, 0)
    kv_pick = kv_items[safe_ids]
    kv_back = lax.all_to_all(
        kv_pick.reshape(seq_devices, slot_cap, 2, blk_size, head_size),
        "seq",
        split_axis=0,
        concat_axis=0,
        tiled=True,
    ).reshape(slot_count, 2, blk_size, head_size)
    rand_kv = kv_back[slot_of_req].reshape(
        heads_here, blk_count, rand_count, 2, blk_size, head_size
    )

    def fixed_list(which):
        own = heads_first(kv_rows[which])
        parts = [own[:, :, None], own[:, ::-1, None]]
        parts += [heads_first(far_arr[which])[:, :, None] for far_arr in far_kv]
        return jnp.concatenate(parts, axis=2)

    key_fix = fixed_list(0)
    value_fix = fixed_list(1)
    key_rnd = rand_kv[:, :, :, 0]
    value_rnd = rand_kv[:, :, :, 1]
    query_h = heads_first(queries)
    grad_h = heads_first(out_grad)

    def mm_scores(rows, key_part):
        return jnp.einsum("hbtd,hbksd->hbtks", rows, key_part, preferred_element_type=f32)

    def mm_out(weight_part, key_part):
        return jnp.einsum("hbtks,hbksd->hbtd", weight_part, key_part, preferred_element_type=f32)

    def mm_terms(weight_part, rows):
        return jnp.einsum("hbtks,hbtd->hbksd", weight_part, rows, preferred_element_type=f32)

    scores_fix = mm_scores(query_h, key_fix) * score_scale
    scores_rnd = mm_scores(query_h, key_rnd) * score_scale
    grad_weights_fix = mm_scores(grad_h, value_fix)
    grad_weights_rnd = mm_scores(grad_h, value_rnd)
    row_max = jnp.maximum(jnp.max(scores_fix, axis=(3, 4)), jnp.max(scores_rnd, axis=(3, 4)))
    exp_sum = jnp.sum(jnp.exp(scores_fix - row_max[..., None, None]), axis=(3, 4)) + jnp.sum(
        jnp.exp(scores_rnd - row_max[..., None, None]), axis=(3, 4)
    )
    log_total = row_max + jnp.log(exp_sum)
    weights_fix = jnp.exp(scores_fix - log_total[..., None, None])
    weights_rnd = jnp.exp(scores_rnd - log_total[..., None, None])
    low_fix = weights_fix.astype(jnp.bfloat16)
    low_rnd = weights_rnd.astype(jnp.bfloat16)
    attn_h = (mm_out(low_fix, value_fix) + mm_out(low_rnd, value_rnd)).astype(jnp.bfloat16)
    row_delta = jnp.sum(grad_h.astype(f32) * attn_h.astype(f32), axis=3)
    grad_scores_fix = (weights_fix * (grad_weights_fix - row_delta[..., None, None])).astype(
        jnp.bfloat16
    )
    grad_scores_rnd = (weights_rnd * (grad_weights_rnd - row_delta[..., None, None])).astype(
        jnp.bfloat16
    )

    rand_low = jnp.stack(
        [score_scale * mm_terms(grad_scores_rnd, query_h), mm_terms(low_rnd, grad_h)]
    ).astype(jnp.bfloat16)
    rand_req = rand_low.transpose(1, 2, 3, 0, 4, 5).reshape(total_req, 2, blk_size, head_size)
    rand_req = jnp.concatenate([rand_req, jnp.zeros_like(rand_req[:1])], axis=0)
    req_of_slot = jnp.where(
        jnp.any(slot_match, axis=1),
        jnp.sum(jnp.where(slot_match, req_index[None, :], 0), axis=1),
        total_req,
    )
    send_terms = rand_req[req_of_slot]
    row_major = Layout(major_to_minor=(0, 1, 2, 3, 4))
    slot_terms = lax.all_to_all(
        with_layout_constraint(
            send_terms.reshape(seq_devices, slot_cap, 2, blk_size, head_size), row_major
        ),
        "seq",
        split_axis=0,
        concat_axis=0,
        tiled=True,
    )
    slot_terms = with_layout_constraint(slot_terms, row_major).reshape(
        slot_count, 2, blk_size, head_size
    )

    grad_query_h = (
        score_scale * (mm_out(grad_scores_fix, key_fix) + mm_out(grad_scores_rnd, key_rnd))
    ).astype(jnp.bfloat16)
    terms = jnp.stack(
        [score_scale * mm_terms(grad_scores_fix, query_h), mm_terms(low_fix, grad_h)]
    )

    grad_kv = terms[:, :, :, 0] + low(terms[:, :, :, 1])[:, :, ::-1]
    far_low = terms[:, :, :, 2:].astype(jnp.bfloat16)
    slow_first = [0, 1, 4, 5, 3, 2] if far_count == 6 else list(range(far_count))
    for far_level in slow_first:
        back = swapped(far_low[:, :, :, far_level], "seq", far_level)
        grad_kv = grad_kv + back.astype(f32)
    grad_rows = grad_kv.transpose(0, 2, 3, 1, 4)

    target_rows = jnp.arange(heads_here * blk_count, dtype=jnp.int32)
    onehot = (asked_flat[None, :] == target_rows[:, None]).astype(jnp.bfloat16)
    extra = jnp.einsum("tp,pksd->tksd", onehot, slot_terms, preferred_element_type=f32)
    extra = extra.reshape(heads_here, blk_count, 2, blk_size, head_size).transpose(2, 1, 3, 0, 4)
    grad_kv = (grad_rows + extra).astype(jnp.bfloat16).reshape(2, tok_rows, heads_here * head_size)

    attn_out = rows_back(attn_h)
    grad_queries = rows_back(grad_query_h)
    grad_keys = grad_kv[0]
    grad_values = grad_kv[1]
    return (attn_out, grad_queries, grad_keys, grad_values)


def solution(mesh):
    return jax.shard_map(
        body,
        mesh=mesh,
        in_specs=(
            P("seq", "head"),
            P("seq", "head"),
            P("seq", "head"),
            P("seq", "head"),
            P("head", "seq", None),
        ),
        out_specs=(P("seq", "head"), P("seq", "head"), P("seq", "head"), P("seq", "head")),
        check_vma=False,
    )
```
